128 devices in a mesh: row: 64 (over z, y, x), col: 2 (over core).
Axes of the slice: x: 4, y: 4, z: 4, core: 2. Of those that a mesh axis runs over, the one named last changes fastest.
Arguments:
- rhs: float32 [2, 64, 1024, 1024], P(None, 'row', None, 'col'), may hold values from -8 to 8
- panels: float32 [2, 2, 64, 1024, 1024], P(None, None, 'row', None, 'col'), may hold values from -0.1875 to 0.1875
- inverses: float32 [2, 1024, 1024], replicated, may hold values from -1 to 4, as said below
Outputs:
- result: float32 [2, 64, 1024, 1024], P(None, 'row', None, 'col')
The draws below stay inside these ranges and needn't reach their ends.
Inputs may be any that keep to these rules, and one draw needn't show every extreme that they name: Each inverses[k] is lower triangular with a positive diagonal.
All inputs are finite; a program needn't handle non-finite values.
Results may differ from the reference program's by a relative error of at most 0.000075.
Values sent between devices are 32-bit elements; how exact they have to be, the bound alone decides.
No kernel may reach another device: no remote copies, remote signals or barrier semaphores. Data moves between devices by JAX's collectives and lax.ppermute only.
A program may use at most 128 MiB of HBM per device.

```python
import math
import jax
import jax.numpy as jnp
from jax import lax

NB = 1024
R = 1024
RBD = 2
N_ROW = 64


def draw_inverses(key, part):
    key_diag, key_off = jax.random.split(jax.random.fold_in(key, 7))
    lower_mask = (jnp.arange(NB)[:, None] > jnp.arange(NB)[None, :]).astype(jnp.float32)
    diagonal = jnp.exp(jax.random.uniform(key_diag, (2, NB), jnp.float32, -math.log(2.0), math.log(2.0)))
    off_diag = jax.random.normal(key_off, (2, NB, NB), jnp.float32) * (0.6 / math.sqrt(NB))
    return off_diag * lower_mask[None] + jnp.eye(NB, dtype=jnp.float32)[None] * diagonal[:, :, None]


def block_scale(rng, shape, shards, smallest, top_value):
    factor_of = 1.0
    for axis_at, shards_of in shards:
        draws = jax.random.uniform(jax.random.fold_in(jax.random.fold_in(rng, 6), axis_at), (shards_of,), jnp.float32, smallest / len(shards), top_value / len(shards))
        factor_of = factor_of * jnp.repeat(jnp.exp(draws), shape[axis_at] // shards_of).reshape((-1,) + (1,) * (len(shape) - 1 - axis_at))
    return factor_of


def noise(key, shape, width, reach, pieces=(), held_as=jnp.bfloat16):
    values = jax.random.normal(key, shape, jnp.float32) * width
    if len(pieces) > 0:
        values = block_scale(key, shape, pieces, -0.22, 0.18) * values
    return jnp.clip(values, min=-reach, max=reach).astype(held_as)


def setup_inputs(seed: int = 0) -> dict:
    arg_keys = jax.random.split(jax.random.key(seed), 4)
    return {
        "rhs": noise(arg_keys[0], (RBD, N_ROW, NB, R), 1.0, 8.0, ((1, 64), (3, 2)), jnp.float32),
        "panels": noise(arg_keys[1], (2, RBD, N_ROW, NB, NB), NB ** -0.5, 0.1875, ((2, 64), (4, 2)), jnp.float32),
        "inverses": draw_inverses(jax.random.fold_in(arg_keys[3], 71), 0),
    }


def reference(rhs, panels, inverses):
    highest = lax.Precision.HIGHEST
    block_ids = (jnp.arange(RBD, dtype=jnp.int32)[:, None] * N_ROW + jnp.arange(N_ROW, dtype=jnp.int32)[None, :])[:, :, None, None]
    solved0 = jnp.dot(inverses[0], rhs[0, 0], precision=highest, preferred_element_type=jnp.float32)
    update0 = jnp.einsum("sqin,nr->sqir", panels[0], solved0, precision=highest, preferred_element_type=jnp.float32)
    sectioned = jnp.where(block_ids >= 1, rhs - update0, solved0)
    solved1 = jnp.dot(inverses[1], sectioned[0, 1], precision=highest, preferred_element_type=jnp.float32)
    update1 = jnp.einsum("sqin,nr->sqir", panels[1], solved1, precision=highest, preferred_element_type=jnp.float32)
    updated = sectioned - update1
    return jnp.where(block_ids >= 2, updated, jnp.where(block_ids == 1, solved1, sectioned))
```

```python
import jax
import jax.numpy as jnp
from jax import lax
from jax.sharding import PartitionSpec as P


def per_device(rhs, panels, inverses):
    highest = lax.Precision.HIGHEST
    row_index = lax.axis_index("row")
    row_count = lax.axis_size("row")
    slot_count = rhs.shape[0]
    block_ids = (jnp.arange(slot_count, dtype=jnp.int32) * row_count + row_index)[
        :, None, None, None
    ]

    def dot(a, b):
        return jnp.dot(a, b, precision=highest, preferred_element_type=jnp.float32)

    wanted = jnp.stack([rhs[0, 0], rhs[0, 0], panels[0, 0, 0]])
    owner = jnp.array([0, 1, 1], dtype=jnp.int32)[:, None, None]
    spread = lax.psum(jnp.where(owner == row_index, wanted, 0).astype(wanted.dtype), "row")
    rhs0, rhs1, tile_half = spread[0], spread[1], spread[2]

    def apply_panel(tiles, solved):
        return jnp.einsum(
            "sqin,nr->sqir",
            lax.all_gather(tiles, "col", axis=3, tiled=True),
            solved,
            precision=highest,
            preferred_element_type=jnp.float32,
        )

    solved0 = dot(inverses[0], rhs0)
    sectioned = rhs - apply_panel(panels[0], solved0)
    sectioned = jnp.where(block_ids >= 1, sectioned, solved0)
    tile = lax.all_gather(tile_half, "col", axis=1, tiled=True)
    solved1 = dot(inverses[1], rhs1 - dot(tile, solved0))
    updated = sectioned - apply_panel(panels[1], solved1)
    return jnp.where(block_ids >= 2, updated, jnp.where(block_ids == 1, solved1, sectioned))


def solution(mesh):
    placed = (P(None, "row", None, "col"), P(None, None, "row", None, "col"), P())
    return jax.shard_map(
        per_device,
        mesh=mesh,
        in_specs=placed,
        out_specs=P(None, "row", None, "col"),
        check_vma=False,
    )
```

```python
import jax
import jax.numpy as jnp
from jax import lax
from jax.sharding import PartitionSpec as P


def per_device(rhs, panels, inverses):
    highest = lax.Precision.HIGHEST
    row_index = lax.axis_index("row")
    row_count = lax.axis_size("row")
    col_index = lax.axis_index("col")
    slot_count = rhs.shape[0]
    half = panels.shape[-1]
    block_ids = (jnp.arange(slot_count, dtype=jnp.int32) * row_count + row_index)[
        :, None, None, None
    ]
    swap = [(0, 1), (1, 0)]

    def dot(a, b):
        return jnp.dot(a, b, precision=highest, preferred_element_type=jnp.float32)

    other_panels = lax.ppermute(panels, "col", swap)

    wanted = jnp.stack([rhs[0, 0], rhs[0, 0], panels[0, 0, 0]])
    owner = jnp.array([0, 1, 1], dtype=jnp.int32)[:, None, None]
    spread = lax.psum(jnp.where(owner == row_index, wanted, 0).astype(wanted.dtype), "row")
    rhs0, rhs1, tile_mine = spread[0], spread[1], spread[2]
    tile_other = lax.ppermute(tile_mine, "col", swap)

    def rows_of(solved, which):
        return lax.dynamic_slice_in_dim(solved, which * half, half, axis=0)

    def split_product(mine, other, solved, spec):
        a = jnp.einsum(spec, mine, rows_of(solved, col_index), precision=highest,
                       preferred_element_type=jnp.float32)
        b = jnp.einsum(spec, other, rows_of(solved, 1 - col_index), precision=highest,
                       preferred_element_type=jnp.float32)
        return a + b

    panel_spec = "sqin,nr->sqir"
    solved0 = dot(inverses[0], rhs0)
    sectioned = rhs - split_product(panels[0], other_panels[0], solved0, panel_spec)
    sectioned = jnp.where(block_ids >= 1, sectioned, solved0)
    solved1 = dot(inverses[1], rhs1 - split_product(tile_mine, tile_other, solved0, "in,nr->ir"))
    updated = sectioned - split_product(panels[1], other_panels[1], solved1, panel_spec)
    return jnp.where(block_ids >= 2, updated, jnp.where(block_ids == 1, solved1, sectioned))


def solution(mesh):
    placed = (P(None, "row", None, "col"), P(None, None, "row", None, "col"), P())
    return jax.shard_map(
        per_device,
        mesh=mesh,
        in_specs=placed,
        out_specs=P(None, "row", None, "col"),
        check_vma=False,
    )
```

```python
import jax
import jax.numpy as jnp
from jax import lax
from jax.sharding import PartitionSpec as P


def per_device(rhs, panels, inverses):
    highest = lax.Precision.HIGHEST
    row_index = lax.axis_index("row")
    row_count = lax.axis_size("row")
    col_index = lax.axis_index("col")
    slot_count = rhs.shape[0]
    half = panels.shape[-1]
    block_ids = (jnp.arange(slot_count, dtype=jnp.int32) * row_count + row_index)[
        :, None, None, None
    ]
    swap = [(0, 1), (1, 0)]

    def dot(a, b):
        return jnp.dot(a, b, precision=highest, preferred_element_type=jnp.float32)

    other_panels = lax.ppermute(panels, "col", swap)

    wanted = jnp.stack([rhs[0, 0], rhs[0, 0], panels[0, 0, 0]])
    owner = jnp.array([0, 1, 1], dtype=jnp.int32)[:, None, None]
    spread = lax.psum(jnp.where(owner == row_index, wanted, 0).astype(wanted.dtype), "row")
    rhs0, rhs1, tile_mine = spread[0], spread[1], spread[2]
    tile_other = lax.ppermute(tile_mine, "col", swap)

    def rows_of(solved, which):
        return lax.dynamic_slice_in_dim(solved, which * half, half, axis=0)

    def split_product(mine, other, solved, spec, precision):
        a = jnp.einsum(spec, mine, rows_of(solved, col_index), precision=precision,
                       preferred_element_type=jnp.float32)
        b = jnp.einsum(spec, other, rows_of(solved, 1 - col_index), precision=precision,
                       preferred_element_type=jnp.float32)
        return a + b

    panel_spec = "sqin,nr->sqir"
    high = lax.Precision.HIGH
    solved0 = dot(inverses[0], rhs0)
    sectioned = rhs - split_product(panels[0], other_panels[0], solved0, panel_spec, high)
    sectioned = jnp.where(block_ids >= 1, sectioned, solved0)
    solved1 = dot(inverses[1], rhs1 - split_product(tile_mine, tile_other, solved0, "in,nr->ir", highest))
    updated = sectioned - split_product(panels[1], other_panels[1], solved1, panel_spec, high)
    return jnp.where(block_ids >= 2, updated, jnp.where(block_ids == 1, solved1, sectioned))


def solution(mesh):
    placed = (P(None, "row", None, "col"), P(None, None, "row", None, "col"), P())
    return jax.shard_map(
        per_device,
        mesh=mesh,
        in_specs=placed,
        out_specs=P(None, "row", None, "col"),
        check_vma=False,
    )
```

```python
import jax
import jax.numpy as jnp
from jax import lax
from jax.sharding import PartitionSpec as P


def per_device(rhs, panels, inverses):
    highest = lax.Precision.HIGHEST
    row_index = lax.axis_index("row")
    row_count = lax.axis_size("row")
    col_index = lax.axis_index("col")
    slot_count = rhs.shape[0]
    half = panels.shape[-1]
    block_ids = (jnp.arange(slot_count, dtype=jnp.int32) * row_count + row_index)[
        :, None, None, None
    ]
    swap = [(0, 1), (1, 0)]

    def dot(a, b):
        return jnp.dot(a, b, precision=highest, preferred_element_type=jnp.float32)

    other_panels = lax.ppermute(panels, "col", swap)

    wanted = jnp.stack([rhs[0, 0], rhs[0, 0], panels[0, 0, 0]])
    owner = jnp.array([0, 1, 1], dtype=jnp.int32)[:, None, None]
    spread = lax.psum(jnp.where(owner == row_index, wanted, 0).astype(wanted.dtype), "row")
    rhs0, rhs1, tile_mine = spread[0], spread[1], spread[2]
    tile_other = lax.ppermute(tile_mine, "col", swap)

    def rows_of(solved, which):
        return lax.dynamic_slice_in_dim(solved, which * half, half, axis=0)

    def split_product(mine, other, solved, precision):
        def product(tiles, which):
            flat = tiles.reshape(-1, tiles.shape[-1])
            out = jnp.dot(flat, rows_of(solved, which), precision=precision,
                          preferred_element_type=jnp.float32)
            return out.reshape(tiles.shape[:-1] + solved.shape[-1:])

        return product(mine, col_index) + product(other, 1 - col_index)

    high = lax.Precision.HIGH
    solved0 = dot(inverses[0], rhs0)
    sectioned = rhs - split_product(panels[0], other_panels[0], solved0, high)
    sectioned = jnp.where(block_ids >= 1, sectioned, solved0)
    solved1 = dot(inverses[1], rhs1 - split_product(tile_mine, tile_other, solved0, highest))
    updated = sectioned - split_product(panels[1], other_panels[1], solved1, high)
    return jnp.where(block_ids >= 2, updated, jnp.where(block_ids == 1, solved1, sectioned))


def solution(mesh):
    placed = (P(None, "row", None, "col"), P(None, None, "row", None, "col"), P())
    return jax.shard_map(
        per_device,
        mesh=mesh,
        in_specs=placed,
        out_specs=P(None, "row", None, "col"),
        check_vma=False,
    )
```

```python
import jax
import jax.numpy as jnp
from jax import lax
from jax.sharding import PartitionSpec as P


def per_device(rhs, panels, inverses):
    highest = lax.Precision.HIGH
    high = highest
    row_index = lax.axis_index("row")
    row_count = lax.axis_size("row")
    col_index = lax.axis_index("col")
    slot_count = rhs.shape[0]
    half = panels.shape[-1]
    block_ids = (jnp.arange(slot_count, dtype=jnp.int32) * row_count + row_index)[
        :, None, None, None
    ]
    swap = [(0, 1), (1, 0)]

    def dot(a, b):
        return jnp.dot(a, b, precision=highest, preferred_element_type=jnp.float32)

    other_panels = lax.ppermute(panels, "col", swap)

    wanted = jnp.stack([rhs[0, 0], rhs[0, 0], panels[0, 0, 0]])
    owner = jnp.array([0, 1, 1], dtype=jnp.int32)[:, None, None]
    spread = lax.psum(jnp.where(owner == row_index, wanted, 0).astype(wanted.dtype), "row")
    rhs0, rhs1, tile_mine = spread[0], spread[1], spread[2]
    tile_other = lax.ppermute(tile_mine, "col", swap)

    def rows_of(solved, which):
        return lax.dynamic_slice_in_dim(solved, which * half, half, axis=0)

    def split_product(mine, other, solved, spec, precision):
        a = jnp.einsum(spec, mine, rows_of(solved, col_index), precision=precision,
                       preferred_element_type=jnp.float32)
        b = jnp.einsum(spec, other, rows_of(solved, 1 - col_index), precision=precision,
                       preferred_element_type=jnp.float32)
        return a + b

    panel_spec = "sqin,nr->sqir"
    solved0 = dot(inverses[0], rhs0)
    sectioned = rhs - split_product(panels[0], other_panels[0], solved0, panel_spec, high)
    sectioned = jnp.where(block_ids >= 1, sectioned, solved0)
    solved1 = dot(inverses[1], rhs1 - split_product(tile_mine, tile_other, solved0, "in,nr->ir", highest))
    updated = sectioned - split_product(panels[1], other_panels[1], solved1, panel_spec, high)
    return jnp.where(block_ids >= 2, updated, jnp.where(block_ids == 1, solved1, sectioned))


def solution(mesh):
    placed = (P(None, "row", None, "col"), P(None, None, "row", None, "col"), P())
    return jax.shard_map(
        per_device,
        mesh=mesh,
        in_specs=placed,
        out_specs=P(None, "row", None, "col"),
        check_vma=False,
    )
```

```python
import jax
import jax.numpy as jnp
from jax import lax
from jax.sharding import PartitionSpec as P


def per_device(rhs, panels, inverses):
    highest = lax.Precision.HIGH
    high = highest
    row_index = lax.axis_index("row")
    row_count = lax.axis_size("row")
    col_index = lax.axis_index("col")
    slot_count = rhs.shape[0]
    half = panels.shape[-1]
    block_ids = (jnp.arange(slot_count, dtype=jnp.int32) * row_count + row_index)[
        :, None, None, None
    ]
    swap = [(0, 1), (1, 0)]

    def dot(a, b):
        return jnp.dot(a, b, precision=highest, preferred_element_type=jnp.float32)

    def lower_dot(lower, b):
        h = lower.shape[0] // 2
        top = dot(lower[:h, :h], b[:h])
        return jnp.concatenate([top, dot(lower[h:], b)], axis=0)

    other_panels = lax.ppermute(panels, "col", swap)

    wanted = jnp.stack([rhs[0, 0], rhs[0, 0], panels[0, 0, 0]])
    owner = jnp.array([0, 1, 1], dtype=jnp.int32)[:, None, None]
    spread = lax.psum(jnp.where(owner == row_index, wanted, 0).astype(wanted.dtype), "row")
    rhs0, rhs1, tile_mine = spread[0], spread[1], spread[2]
    tile_other = lax.ppermute(tile_mine, "col", swap)

    def rows_of(solved, which):
        return lax.dynamic_slice_in_dim(solved, which * half, half, axis=0)

    def split_product(mine, other, solved, spec, precision):
        a = jnp.einsum(spec, mine, rows_of(solved, col_index), precision=precision,
                       preferred_element_type=jnp.float32)
        b = jnp.einsum(spec, other, rows_of(solved, 1 - col_index), precision=precision,
                       preferred_element_type=jnp.float32)
        return a + b

    panel_spec = "sqin,nr->sqir"
    solved0 = lower_dot(inverses[0], rhs0)
    sectioned = rhs - split_product(panels[0], other_panels[0], solved0, panel_spec, high)
    sectioned = jnp.where(block_ids >= 1, sectioned, solved0)
    solved1 = lower_dot(inverses[1], rhs1 - split_product(tile_mine, tile_other, solved0, "in,nr->ir", highest))
    updated = sectioned - split_product(panels[1], other_panels[1], solved1, panel_spec, high)
    return jnp.where(block_ids >= 2, updated, jnp.where(block_ids == 1, solved1, sectioned))


def solution(mesh):
    placed = (P(None, "row", None, "col"), P(None, None, "row", None, "col"), P())
    return jax.shard_map(
        per_device,
        mesh=mesh,
        in_specs=placed,
        out_specs=P(None, "row", None, "col"),
        check_vma=False,
    )
```

```python
import jax
import jax.numpy as jnp
from jax import lax
from jax.sharding import PartitionSpec as P


def per_device(rhs, panels, inverses):
    highest = lax.Precision.HIGH
    high = highest
    row_index = lax.axis_index("row")
    row_count = lax.axis_size("row")
    col_index = lax.axis_index("col")
    slot_count = rhs.shape[0]
    half = panels.shape[-1]
    block_ids = (jnp.arange(slot_count, dtype=jnp.int32) * row_count + row_index)[
        :, None, None, None
    ]
    swap = [(0, 1), (1, 0)]

    def dot(a, b):
        return jnp.dot(a, b, precision=highest, preferred_element_type=jnp.float32)

    other_panels = lax.ppermute(panels, "col", swap)

    wanted = jnp.stack([rhs[0, 0], rhs[0, 0], panels[0, 0, 0]])
    owner = jnp.array([0, 1, 1], dtype=jnp.int32)[:, None, None]
    spread = lax.psum(jnp.where(owner == row_index, wanted, 0).astype(wanted.dtype), "row")

    def rows_of(solved, which):
        return lax.dynamic_slice_in_dim(solved, which * half, half, axis=0)

    def split_product(mine, other, solved, spec, precision):
        a = jnp.einsum(spec, mine, rows_of(solved, col_index), precision=precision,
                       preferred_element_type=jnp.float32)
        b = jnp.einsum(spec, other, rows_of(solved, 1 - col_index), precision=precision,
                       preferred_element_type=jnp.float32)
        return a + b

    high = highest

    def full_product(mine, other, right):
        spec = "sqin,nm->sqim"
        a = jnp.einsum(spec, mine, rows_of(right, col_index), precision=high,
                       preferred_element_type=jnp.float32)
        b = jnp.einsum(spec, other, rows_of(right, 1 - col_index), precision=high,
                       preferred_element_type=jnp.float32)
        return a + b

    first = full_product(panels[0], other_panels[0], inverses[0])
    second = full_product(panels[1], other_panels[1], inverses[1])
    is_row0 = block_ids == 0
    is_row1 = block_ids == 1
    zero = jnp.zeros_like(first)
    first = jnp.where(is_row0, -inverses[0], jnp.where(is_row1, zero, first))
    second = jnp.where(is_row0, zero, jnp.where(is_row1, -inverses[1], second))
    kept = jnp.where(block_ids >= 2, rhs, 0).astype(rhs.dtype)
    spread, first, second, kept = lax.optimization_barrier((spread, first, second, kept))
    rhs0, rhs1, tile_mine = spread[0], spread[1], spread[2]
    tile_other = lax.ppermute(tile_mine, "col", swap)

    solved0 = dot(inverses[0], rhs0)
    sectioned1 = rhs1 - split_product(tile_mine, tile_other, solved0, "in,nr->ir", highest)
    apply = "sqim,mr->sqir"
    out = kept - jnp.einsum(apply, first, rhs0, precision=high, preferred_element_type=jnp.float32)
    return out - jnp.einsum(apply, second, sectioned1, precision=high,
                            preferred_element_type=jnp.float32)


def solution(mesh):
    placed = (P(None, "row", None, "col"), P(None, None, "row", None, "col"), P())
    return jax.shard_map(
        per_device,
        mesh=mesh,
        in_specs=placed,
        out_specs=P(None, "row", None, "col"),
        check_vma=False,
    )
```

```python
import jax
import jax.numpy as jnp
from jax import lax
from jax.sharding import PartitionSpec as P


def per_device(rhs, panels, inverses):
    highest = lax.Precision.HIGH
    high = highest
    row_index = lax.axis_index("row")
    row_count = lax.axis_size("row")
    col_index = lax.axis_index("col")
    slot_count = rhs.shape[0]
    half = panels.shape[-1]
    block_ids = (jnp.arange(slot_count, dtype=jnp.int32) * row_count + row_index)[
        :, None, None, None
    ]
    swap = [(0, 1), (1, 0)]

    def dot(a, b):
        return jnp.dot(a, b, precision=highest, preferred_element_type=jnp.float32)

    other_panels = lax.ppermute(panels, "col", swap)

    wanted = jnp.stack([rhs[0, 0], rhs[0, 0], panels[0, 0, 0]])
    owner = jnp.array([0, 1, 1], dtype=jnp.int32)[:, None, None]
    spread = lax.psum(jnp.where(owner == row_index, wanted, 0).astype(wanted.dtype), "row")

    def rows_of(solved, which):
        return lax.dynamic_slice_in_dim(solved, which * half, half, axis=0)

    def split_product(mine, other, solved, spec, precision):
        a = jnp.einsum(spec, mine, rows_of(solved, col_index), precision=precision,
                       preferred_element_type=jnp.float32)
        b = jnp.einsum(spec, other, rows_of(solved, 1 - col_index), precision=precision,
                       preferred_element_type=jnp.float32)
        return a + b

    high = highest

    def full_product(mine, other, right):
        spec = "sqin,nm->sqim"
        a = jnp.einsum(spec, mine, rows_of(right, col_index), precision=high,
                       preferred_element_type=jnp.float32)
        b = jnp.einsum(spec, other, rows_of(right, 1 - col_index), precision=high,
                       preferred_element_type=jnp.float32)
        return a + b

    first = full_product(panels[0], other_panels[0], inverses[0])
    second = full_product(panels[1], other_panels[1], inverses[1])
    is_row0 = block_ids == 0
    is_row1 = block_ids == 1
    zero = jnp.zeros_like(first)
    first = jnp.where(is_row0, -inverses[0], jnp.where(is_row1, zero, first))
    second = jnp.where(is_row0, zero, jnp.where(is_row1, -inverses[1], second))
    kept = jnp.where(block_ids >= 2, rhs, 0).astype(rhs.dtype)
    spread, first, second, kept = lax.optimization_barrier((spread, first, second, kept))
    rhs0, rhs1, tile_mine = spread[0], spread[1], spread[2]
    tile_other = lax.ppermute(tile_mine, "col", swap)

    solved0 = dot(inverses[0], rhs0)
    sectioned1 = rhs1 - split_product(tile_mine, tile_other, solved0, "in,nr->ir", highest)
    sectioned1 = lax.optimization_barrier(sectioned1)
    apply = "sqim,mr->sqir"
    out = kept - jnp.einsum(apply, first, rhs0, precision=high, preferred_element_type=jnp.float32)
    return out - jnp.einsum(apply, second, sectioned1, precision=high,
                            preferred_element_type=jnp.float32)


def solution(mesh):
    placed = (P(None, "row", None, "col"), P(None, None, "row", None, "col"), P())
    return jax.shard_map(
        per_device,
        mesh=mesh,
        in_specs=placed,
        out_specs=P(None, "row", None, "col"),
        check_vma=False,
    )
```

```python
import jax
import jax.numpy as jnp
from jax import lax
from jax.sharding import PartitionSpec as P


def per_device(rhs, panels, inverses):
    highest = lax.Precision.HIGH
    high = highest
    row_index = lax.axis_index("row")
    row_count = lax.axis_size("row")
    col_index = lax.axis_index("col")
    slot_count = rhs.shape[0]
    half = panels.shape[-1]
    block_ids = (jnp.arange(slot_count, dtype=jnp.int32) * row_count + row_index)[
        :, None, None, None
    ]
    swap = [(0, 1), (1, 0)]

    def dot(a, b):
        return jnp.dot(a, b, precision=highest, preferred_element_type=jnp.float32)

    other_panels = lax.ppermute(panels, "col", swap)

    wanted = jnp.stack([rhs[0, 0], rhs[0, 0], panels[0, 0, 0]])
    owner = jnp.array([0, 1, 1], dtype=jnp.int32)[:, None, None]
    spread = lax.psum(jnp.where(owner == row_index, wanted, 0).astype(wanted.dtype), "row")

    def rows_of(solved, which):
        return lax.dynamic_slice_in_dim(solved, which * half, half, axis=0)

    def split_product(mine, other, solved, spec, precision):
        a = jnp.einsum(spec, mine, rows_of(solved, col_index), precision=precision,
                       preferred_element_type=jnp.float32)
        b = jnp.einsum(spec, other, rows_of(solved, 1 - col_index), precision=precision,
                       preferred_element_type=jnp.float32)
        return a + b

    high = highest

    def full_product(mine, other, right):
        spec = "sqin,nm->sqim"
        a = jnp.einsum(spec, mine, rows_of(right, col_index), precision=high,
                       preferred_element_type=jnp.float32)
        b = jnp.einsum(spec, other, rows_of(right, 1 - col_index), precision=high,
                       preferred_element_type=jnp.float32)
        return a + b

    first = full_product(panels[0], other_panels[0], inverses[0])
    second = full_product(panels[1], other_panels[1], inverses[1])
    is_row0 = block_ids == 0
    is_row1 = block_ids == 1
    zero = jnp.zeros_like(first)
    first = jnp.where(is_row0, -inverses[0], jnp.where(is_row1, zero, first))
    second = jnp.where(is_row0, zero, jnp.where(is_row1, -inverses[1], second))
    kept = jnp.where(block_ids >= 2, rhs, 0).astype(rhs.dtype)
    first = jnp.concatenate([first.reshape((-1,) + first.shape[-2:]), inverses[0][None]])
    spread, first, second, kept = lax.optimization_barrier((spread, first, second, kept))
    rhs0, rhs1, tile_mine = spread[0], spread[1], spread[2]
    tile_other = lax.ppermute(tile_mine, "col", swap)

    firsts = jnp.einsum("kim,mr->kir", first, rhs0, precision=high,
                        preferred_element_type=jnp.float32)
    solved0 = firsts[-1]
    sectioned1 = rhs1 - split_product(tile_mine, tile_other, solved0, "in,nr->ir", highest)
    sectioned1 = lax.optimization_barrier(sectioned1)
    apply = "sqim,mr->sqir"
    out = kept - firsts[:-1].reshape(kept.shape)
    return out - jnp.einsum(apply, second, sectioned1, precision=high,
                            preferred_element_type=jnp.float32)


def solution(mesh):
    placed = (P(None, "row", None, "col"), P(None, None, "row", None, "col"), P())
    return jax.shard_map(
        per_device,
        mesh=mesh,
        in_specs=placed,
        out_specs=P(None, "row", None, "col"),
        check_vma=False,
    )
```

```python
import jax
import jax.numpy as jnp
from jax import lax
from jax.sharding import PartitionSpec as P


def per_device(rhs, panels, inverses):
    highest = lax.Precision.HIGH
    high = highest
    row_index = lax.axis_index("row")
    row_count = lax.axis_size("row")
    col_index = lax.axis_index("col")
    slot_count = rhs.shape[0]
    half = panels.shape[-1]
    block_ids = (jnp.arange(slot_count, dtype=jnp.int32) * row_count + row_index)[
        :, None, None, None
    ]
    swap = [(0, 1), (1, 0)]

    def dot(a, b):
        return jnp.dot(a, b, precision=highest, preferred_element_type=jnp.float32)

    other_panels = lax.ppermute(panels, "col", swap)

    def kept_at(owner, value):
        return jnp.where(row_index == owner, value, 0).astype(value.dtype)

    spread = lax.psum((kept_at(0, rhs[0, 0]), kept_at(1, rhs[0, 0]), kept_at(1, panels[0, 0, 0])), "row")

    def rows_of(solved, which):
        return lax.dynamic_slice_in_dim(solved, which * half, half, axis=0)

    def split_product(mine, other, solved, spec, precision):
        a = jnp.einsum(spec, mine, rows_of(solved, col_index), precision=precision,
                       preferred_element_type=jnp.float32)
        b = jnp.einsum(spec, other, rows_of(solved, 1 - col_index), precision=precision,
                       preferred_element_type=jnp.float32)
        return a + b

    high = highest

    def full_product(mine, other, right):
        spec = "sqin,nm->sqim"
        a = jnp.einsum(spec, mine, rows_of(right, col_index), precision=high,
                       preferred_element_type=jnp.float32)
        b = jnp.einsum(spec, other, rows_of(right, 1 - col_index), precision=high,
                       preferred_element_type=jnp.float32)
        return a + b

    first = full_product(panels[0], other_panels[0], inverses[0])
    second = full_product(panels[1], other_panels[1], inverses[1])
    is_row0 = block_ids == 0
    is_row1 = block_ids == 1
    zero = jnp.zeros_like(first)
    first = jnp.where(is_row0, -inverses[0], jnp.where(is_row1, zero, first))
    second = jnp.where(is_row0, zero, jnp.where(is_row1, -inverses[1], second))
    kept = jnp.where(block_ids >= 2, rhs, 0).astype(rhs.dtype)
    first = jnp.concatenate([first.reshape((-1,) + first.shape[-2:]), inverses[0][None]])
    spread, first, second, kept = lax.optimization_barrier((spread, first, second, kept))
    rhs0, rhs1, tile_mine = spread[0], spread[1], spread[2]
    tile_other = lax.ppermute(tile_mine, "col", swap)

    firsts = jnp.einsum("kim,mr->kir", first, rhs0, precision=high,
                        preferred_element_type=jnp.float32)
    solved0 = firsts[-1]
    sectioned1 = rhs1 - split_product(tile_mine, tile_other, solved0, "in,nr->ir", highest)
    sectioned1 = lax.optimization_barrier(sectioned1)
    apply = "sqim,mr->sqir"
    out = kept - firsts[:-1].reshape(kept.shape)
    return out - jnp.einsum(apply, second, sectioned1, precision=high,
                            preferred_element_type=jnp.float32)


def solution(mesh):
    placed = (P(None, "row", None, "col"), P(None, None, "row", None, "col"), P())
    return jax.shard_map(
        per_device,
        mesh=mesh,
        in_specs=placed,
        out_specs=P(None, "row", None, "col"),
        check_vma=False,
    )
```

```python
import jax
import jax.numpy as jnp
from jax import lax
from jax.sharding import PartitionSpec as P


def per_device(rhs, panels, inverses):
    highest = lax.Precision.HIGH
    high = highest
    row_index = lax.axis_index("row")
    row_count = lax.axis_size("row")
    col_index = lax.axis_index("col")
    slot_count = rhs.shape[0]
    half = panels.shape[-1]
    block_ids = (jnp.arange(slot_count, dtype=jnp.int32) * row_count + row_index)[
        :, None, None, None
    ]
    swap = [(0, 1), (1, 0)]

    def dot(a, b):
        return jnp.dot(a, b, precision=highest, preferred_element_type=jnp.float32)

    other_panels = lax.ppermute(panels, "col", swap)

    def kept_at(owner, value):
        return jnp.where(row_index == owner, value, 0).astype(value.dtype)

    spread = lax.psum((kept_at(0, rhs[0, 0]), kept_at(1, rhs[0, 0]), kept_at(1, panels[0, 0, 0])), "row")

    def rows_of(solved, which):
        return lax.dynamic_slice_in_dim(solved, which * half, half, axis=0)

    def split_product(mine, other, solved, spec, precision):
        a = jnp.einsum(spec, mine, rows_of(solved, col_index), precision=precision,
                       preferred_element_type=jnp.float32)
        b = jnp.einsum(spec, other, rows_of(solved, 1 - col_index), precision=precision,
                       preferred_element_type=jnp.float32)
        return a + b

    high = highest

    whole = jnp.where(
        col_index == 0,
        jnp.concatenate([panels, other_panels], axis=-1),
        jnp.concatenate([other_panels, panels], axis=-1),
    )

    def full_product(tiles, right):
        return jnp.einsum("sqin,nm->sqim", tiles, right, precision=high,
                          preferred_element_type=jnp.float32)

    first = full_product(whole[0], inverses[0])
    second = full_product(whole[1], inverses[1])
    is_row0 = block_ids == 0
    is_row1 = block_ids == 1
    zero = jnp.zeros_like(first)
    first = jnp.where(is_row0, -inverses[0], jnp.where(is_row1, zero, first))
    second = jnp.where(is_row0, zero, jnp.where(is_row1, -inverses[1], second))
    kept = jnp.where(block_ids >= 2, rhs, 0).astype(rhs.dtype)
    first = jnp.concatenate([first.reshape((-1,) + first.shape[-2:]), inverses[0][None]])
    spread, first, second, kept = lax.optimization_barrier((spread, first, second, kept))
    rhs0, rhs1, tile_mine = spread[0], spread[1], spread[2]
    tile_other = lax.ppermute(tile_mine, "col", swap)

    firsts = jnp.einsum("kim,mr->kir", first, rhs0, precision=high,
                        preferred_element_type=jnp.float32)
    solved0 = firsts[-1]
    sectioned1 = rhs1 - split_product(tile_mine, tile_other, solved0, "in,nr->ir", highest)
    sectioned1 = lax.optimization_barrier(sectioned1)
    apply = "sqim,mr->sqir"
    out = kept - firsts[:-1].reshape(kept.shape)
    return out - jnp.einsum(apply, second, sectioned1, precision=high,
                            preferred_element_type=jnp.float32)


def solution(mesh):
    placed = (P(None, "row", None, "col"), P(None, None, "row", None, "col"), P())
    return jax.shard_map(
        per_device,
        mesh=mesh,
        in_specs=placed,
        out_specs=P(None, "row", None, "col"),
        check_vma=False,
    )
```

```python
import jax
import jax.numpy as jnp
from jax import lax
from jax.sharding import PartitionSpec as P


def per_device(rhs, panels, inverses):
    highest = lax.Precision.HIGH
    high = highest
    row_index = lax.axis_index("row")
    row_count = lax.axis_size("row")
    col_index = lax.axis_index("col")
    slot_count = rhs.shape[0]
    half = panels.shape[-1]
    block_ids = (jnp.arange(slot_count, dtype=jnp.int32) * row_count + row_index)[
        :, None, None, None
    ]
    swap = [(0, 1), (1, 0)]

    def dot(a, b):
        return jnp.dot(a, b, precision=highest, preferred_element_type=jnp.float32)

    other_panels = lax.ppermute(panels, "col", swap)

    def kept_at(owner, value):
        return jnp.where(row_index == owner, value, 0).astype(value.dtype)

    spread = lax.psum((kept_at(0, rhs[0, 0]), kept_at(1, rhs[0, 0]), kept_at(1, panels[0, 0, 0])), "row")


    whole = jnp.concatenate([panels, other_panels], axis=-1)

    def mine_first(matrix):
        return jnp.roll(matrix, -col_index * half, axis=0)

    inverse0, inverse1 = mine_first(inverses[0]), mine_first(inverses[1])

    def full_product(tiles, right):
        return jnp.einsum("sqin,nm->sqim", tiles, right, precision=high,
                          preferred_element_type=jnp.float32)

    first = full_product(whole[0], inverse0)
    second = full_product(whole[1], inverse1)
    is_row0 = block_ids == 0
    is_row1 = block_ids == 1
    zero = jnp.zeros_like(first)
    first = jnp.where(is_row0, -inverses[0], jnp.where(is_row1, zero, first))
    second = jnp.where(is_row0, zero, jnp.where(is_row1, -inverses[1], second))
    kept = jnp.where(block_ids >= 2, rhs, 0).astype(rhs.dtype)
    first = jnp.concatenate([first.reshape((-1,) + first.shape[-2:]), inverse0[None]])
    spread, first, second, kept = lax.optimization_barrier((spread, first, second, kept))
    rhs0, rhs1, tile_mine = spread[0], spread[1], spread[2]
    tile_other = lax.ppermute(tile_mine, "col", swap)

    firsts = jnp.einsum("kim,mr->kir", first, rhs0, precision=high,
                        preferred_element_type=jnp.float32)
    solved0 = firsts[-1]
    sectioned1 = rhs1 - dot(jnp.concatenate([tile_mine, tile_other], axis=-1), solved0)
    sectioned1 = lax.optimization_barrier(sectioned1)
    apply = "sqim,mr->sqir"
    out = kept - firsts[:-1].reshape(kept.shape)
    return out - jnp.einsum(apply, second, sectioned1, precision=high,
                            preferred_element_type=jnp.float32)


def solution(mesh):
    placed = (P(None, "row", None, "col"), P(None, None, "row", None, "col"), P())
    return jax.shard_map(
        per_device,
        mesh=mesh,
        in_specs=placed,
        out_specs=P(None, "row", None, "col"),
        check_vma=False,
    )
```

```python
import jax
import jax.numpy as jnp
from jax import lax
from jax.sharding import PartitionSpec as P


def per_device(rhs, panels, inverses):
    highest = lax.Precision.HIGH
    high = highest
    row_index = lax.axis_index("row")
    row_count = lax.axis_size("row")
    col_index = lax.axis_index("col")
    slot_count = rhs.shape[0]
    half = panels.shape[-1]
    block_ids = (jnp.arange(slot_count, dtype=jnp.int32) * row_count + row_index)[
        :, None, None, None
    ]
    swap = [(0, 1), (1, 0)]

    def dot(a, b):
        return jnp.dot(a, b, precision=highest, preferred_element_type=jnp.float32)

    other_panels = lax.ppermute(panels, "col", swap)

    def kept_at(owner, value):
        return jnp.where(row_index == owner, value, 0).astype(value.dtype)

    spread = lax.psum((kept_at(0, rhs[0, 0]), kept_at(1, rhs[0, 0]), kept_at(1, panels[0, 0, 0])), "row")


    whole = jnp.concatenate([panels, other_panels], axis=-1)

    def mine_first(matrix):
        return jnp.roll(matrix, -col_index * half, axis=0)

    inverse0, inverse1 = mine_first(inverses[0]), mine_first(inverses[1])

    def full_product(tiles, right):
        return jnp.einsum("sqin,nm->sqim", tiles, right, precision=high,
                          preferred_element_type=jnp.float32)

    first = full_product(whole[0], inverse0)
    second = full_product(whole[1], inverse1)
    is_row0 = block_ids == 0
    is_row1 = block_ids == 1
    zero = jnp.zeros_like(first)
    first = jnp.where(is_row0, inverses[0], jnp.where(is_row1, zero, -first))
    second = jnp.where(is_row0, zero, jnp.where(is_row1, -inverses[1], second))
    kept = jnp.where(block_ids >= 2, rhs, 0).astype(rhs.dtype)
    first = jnp.concatenate([first.reshape((-1,) + first.shape[-2:]), inverse0[None]])
    kept = jnp.concatenate([kept.reshape((-1,) + kept.shape[-2:]), jnp.zeros_like(kept[0, 0])[None]])
    spread, first, second, kept = lax.optimization_barrier((spread, first, second, kept))
    rhs0, rhs1, tile_mine = spread[0], spread[1], spread[2]
    tile_other = lax.ppermute(tile_mine, "col", swap)

    firsts = kept + jnp.einsum("kim,mr->kir", first, rhs0, precision=high,
                               preferred_element_type=jnp.float32)
    solved0 = firsts[-1]
    sectioned1 = rhs1 - dot(jnp.concatenate([tile_mine, tile_other], axis=-1), solved0)
    sectioned1 = lax.optimization_barrier(sectioned1)
    apply = "sqim,mr->sqir"
    out = firsts[:-1].reshape(rhs.shape)
    return out - jnp.einsum(apply, second, sectioned1, precision=high,
                            preferred_element_type=jnp.float32)


def solution(mesh):
    placed = (P(None, "row", None, "col"), P(None, None, "row", None, "col"), P())
    return jax.shard_map(
        per_device,
        mesh=mesh,
        in_specs=placed,
        out_specs=P(None, "row", None, "col"),
        check_vma=False,
    )
```

```python
import jax
import jax.numpy as jnp
from jax import lax
from jax.sharding import PartitionSpec as P


def per_device(rhs, panels, inverses):
    highest = lax.Precision.HIGH
    high = highest
    row_index = lax.axis_index("row")
    row_count = lax.axis_size("row")
    col_index = lax.axis_index("col")
    slot_count = rhs.shape[0]
    half = panels.shape[-1]
    block_ids = (jnp.arange(slot_count, dtype=jnp.int32) * row_count + row_index)[
        :, None, None, None
    ]
    swap = [(0, 1), (1, 0)]

    def dot(a, b):
        return jnp.dot(a, b, precision=highest, preferred_element_type=jnp.float32)

    other_panels = lax.ppermute(panels, "col", swap)

    def kept_at(owner, value):
        return value * (row_index == owner).astype(value.dtype)

    spread = lax.psum((kept_at(0, rhs[0, 0]), kept_at(1, rhs[0, 0]), kept_at(1, panels[0, 0, 0])), "row")


    whole = jnp.concatenate([panels, other_panels], axis=-1)

    def mine_first(matrix):
        return jnp.roll(matrix, -col_index * half, axis=0)

    inverse0, inverse1 = mine_first(inverses[0]), mine_first(inverses[1])

    def full_product(tiles, right):
        return jnp.einsum("sqin,nm->sqim", tiles, right, precision=high,
                          preferred_element_type=jnp.float32)

    first = full_product(whole[0], inverse0)
    second = full_product(whole[1], inverse1)
    is_row0 = block_ids == 0
    is_row1 = block_ids == 1
    zero = jnp.zeros_like(first)
    first = jnp.where(is_row0, -inverses[0], jnp.where(is_row1, zero, first))
    second = jnp.where(is_row0, zero, jnp.where(is_row1, -inverses[1], second))
    kept = jnp.where(block_ids >= 2, rhs, 0).astype(rhs.dtype)
    first = jnp.concatenate([first.reshape((-1,) + first.shape[-2:]), inverse0[None]])
    spread, first, second, kept = lax.optimization_barrier((spread, first, second, kept))
    rhs0, rhs1, tile_mine = spread[0], spread[1], spread[2]
    tile_other = lax.ppermute(tile_mine, "col", swap)

    firsts = jnp.einsum("kim,mr->kir", first, rhs0, precision=high,
                        preferred_element_type=jnp.float32)
    solved0 = firsts[-1]
    sectioned1 = rhs1 - dot(jnp.concatenate([tile_mine, tile_other], axis=-1), solved0)
    sectioned1 = lax.optimization_barrier(sectioned1)
    apply = "sqim,mr->sqir"
    out = kept - firsts[:-1].reshape(kept.shape)
    return out - jnp.einsum(apply, second, sectioned1, precision=high,
                            preferred_element_type=jnp.float32)


def solution(mesh):
    placed = (P(None, "row", None, "col"), P(None, None, "row", None, "col"), P())
    return jax.shard_map(
        per_device,
        mesh=mesh,
        in_specs=placed,
        out_specs=P(None, "row", None, "col"),
        check_vma=False,
    )
```

```python
import jax
import jax.numpy as jnp
from jax import lax
from jax.sharding import PartitionSpec as P


def per_device(rhs, panels, inverses):
    highest = lax.Precision.HIGH
    high = highest
    row_index = lax.axis_index("row")
    row_count = lax.axis_size("row")
    col_index = lax.axis_index("col")
    slot_count = rhs.shape[0]
    half = panels.shape[-1]
    block_ids = (jnp.arange(slot_count, dtype=jnp.int32) * row_count + row_index)[
        :, None, None, None
    ]
    swap = [(0, 1), (1, 0)]

    def dot(a, b):
        return jnp.dot(a, b, precision=highest, preferred_element_type=jnp.float32)

    other_panels = lax.ppermute(panels, "col", swap)

    def kept_at(owner, value):
        return value * (row_index == owner).astype(value.dtype)

    spread = lax.psum((kept_at(0, rhs[0, 0]), kept_at(1, rhs[0, 0]), kept_at(1, panels[0, 0, 0])), "row")


    whole = jnp.concatenate([panels, other_panels], axis=-1)

    def mine_first(matrix):
        return jnp.roll(matrix, -col_index * half, axis=0)

    inverse0, inverse1 = mine_first(inverses[0]), mine_first(inverses[1])

    def full_product(tiles, right):
        return jnp.einsum("sqin,nm->sqim", tiles, right, precision=high,
                          preferred_element_type=jnp.float32)

    first = full_product(whole[0], inverse0)
    second = full_product(whole[1], inverse1)
    is_row0 = block_ids == 0
    is_row1 = block_ids == 1
    zero = jnp.zeros_like(first)
    first = jnp.where(is_row0, -inverses[0], jnp.where(is_row1, zero, first))
    second = jnp.where(is_row0, zero, jnp.where(is_row1, -inverses[1], second))
    kept = jnp.where(block_ids >= 2, rhs, 0).astype(rhs.dtype)
    first = jnp.concatenate([first.reshape((-1,) + first.shape[-2:]), inverse0[None]])
    spread, first, second, kept = lax.optimization_barrier((spread, first, second, kept))
    rhs0, rhs1, tile_mine = spread[0], spread[1], spread[2]
    tile_other = lax.ppermute(tile_mine, "col", swap)

    firsts = jnp.einsum("kim,mr->kir", first, rhs0, precision=high,
                        preferred_element_type=jnp.float32)
    solved0 = firsts[-1]
    sectioned1 = rhs1 - dot(jnp.concatenate([tile_mine, tile_other], axis=-1), solved0)
    apply = "sqim,mr->sqir"
    out = kept - firsts[:-1].reshape(kept.shape)
    return out - jnp.einsum(apply, second, sectioned1, precision=high,
                            preferred_element_type=jnp.float32)


def solution(mesh):
    placed = (P(None, "row", None, "col"), P(None, None, "row", None, "col"), P())
    return jax.shard_map(
        per_device,
        mesh=mesh,
        in_specs=placed,
        out_specs=P(None, "row", None, "col"),
        check_vma=False,
    )
```

```python
import jax
import jax.numpy as jnp
from jax import lax
from jax.sharding import PartitionSpec as P


def per_device(rhs, panels, inverses):
    highest = lax.Precision.HIGH
    high = highest
    row_index = lax.axis_index("row")
    row_count = lax.axis_size("row")
    col_index = lax.axis_index("col")
    slot_count = rhs.shape[0]
    half = panels.shape[-1]
    block_ids = (jnp.arange(slot_count, dtype=jnp.int32) * row_count + row_index)[
        :, None, None, None
    ]
    swap = [(0, 1), (1, 0)]

    def dot(a, b):
        return jnp.dot(a, b, precision=highest, preferred_element_type=jnp.float32)

    other_panels = lax.ppermute(panels, "col", swap)

    def kept_at(owner, value):
        return value * (row_index == owner).astype(value.dtype)

    spread = lax.psum((kept_at(0, rhs[0, 0]), kept_at(1, rhs[0, 0]), kept_at(1, panels[0, 0, 0])), "row")


    whole = jnp.concatenate([panels, other_panels], axis=-1)

    def mine_first(matrix):
        return jnp.roll(matrix, -col_index * half, axis=0)

    inverse0, inverse1 = mine_first(inverses[0]), mine_first(inverses[1])

    def full_product(tiles, right):
        return jnp.einsum("sqin,nm->sqim", tiles, right, precision=high,
                          preferred_element_type=jnp.float32)

    first = full_product(whole[0], inverse0)
    second = full_product(whole[1], inverse1)
    is_row0 = block_ids == 0
    is_row1 = block_ids == 1
    zero = jnp.zeros_like(first)
    first = jnp.where(is_row0, -inverses[0], jnp.where(is_row1, zero, first))
    second = jnp.where(is_row0, zero, jnp.where(is_row1, -inverses[1], second))
    kept = jnp.where(block_ids >= 2, rhs, 0).astype(rhs.dtype)
    both = jnp.concatenate([first, second], axis=-1)
    spread, both, inverse0, kept = lax.optimization_barrier((spread, both, inverse0, kept))
    rhs0, rhs1, tile_mine = spread[0], spread[1], spread[2]
    tile_other = lax.ppermute(tile_mine, "col", swap)

    solved0 = dot(inverse0, rhs0)
    sectioned1 = rhs1 - dot(jnp.concatenate([tile_mine, tile_other], axis=-1), solved0)
    stacked = jnp.concatenate([rhs0, sectioned1], axis=0)
    return kept - jnp.einsum("sqim,mr->sqir", both, stacked, precision=high,
                             preferred_element_type=jnp.float32)


def solution(mesh):
    placed = (P(None, "row", None, "col"), P(None, None, "row", None, "col"), P())
    return jax.shard_map(
        per_device,
        mesh=mesh,
        in_specs=placed,
        out_specs=P(None, "row", None, "col"),
        check_vma=False,
    )
```
